256 devices in a mesh: sa: 8 (over z), sb: 4 (over y_lo, core), sl: 8 (over x, y_hi).
Axes of the slice: x: 4, y: 4 (y_hi: 2, y_lo: 2; y = y_hi * 2 + y_lo), z: 8, core: 2. Of those that a mesh axis runs over, the one named last changes fastest.
Arguments:
- stem_cache: bfloat16 [256, 2, 128, 4096], P(('sa', 'sb', 'sl')), may hold values from -6 to 6
- subtree_cache: bfloat16 [256, 2, 4096, 512], P(('sa', 'sb', 'sl')), may hold values from -0.0625 to 0.0625
- final_gates: bfloat16 [2, 512, 512], replicated, may hold values from -0.01171875 to 0.01171875
- group_rows: int32 [32], replicated, may hold values from 0 to 7
Outputs:
- amplitudes: float32 [512, 1024], P(('sa', 'sb', 'sl'))
The draws below stay inside these ranges and needn't reach their ends.
All inputs are finite; a program needn't handle non-finite values.
Results may differ from the reference program's by a relative error of at most 0.0029.
Values may be sent and summed in bfloat16 or wider, within the bound.
No kernel may reach another device: no remote copies, remote signals or barrier semaphores. Data moves between devices by JAX's collectives and lax.ppermute only.
A program may use at most 64 MiB of HBM per device.

```python
import jax
import jax.numpy as jnp
from jax import lax

K = 4096
N = 512
M = 128
RB = 16
G = 32
R = 512
SLICES = 256
N_SA = 8
N_SB = 4
N_SL = 8


def with_ends(values, stream_key, smallest, high):
    place = [jax.random.randint(jax.random.fold_in(stream_key, axis), (), 0, length) for axis, length in enumerate(values.shape)]
    longest = values.shape.index(max(values.shape))
    beside = place[:longest] + [(place[longest] + 1) % values.shape[longest]] + place[longest + 1:]
    return values.at[tuple(place)].set(smallest).at[tuple(beside)].set(high)


def level_of(own_key, shape, split, smallest, largest):
    loudness = 1.0
    for dim, parts in split:
        draws = jax.random.uniform(jax.random.fold_in(jax.random.fold_in(own_key, 6), dim), (parts,), jnp.float32, smallest / len(split), largest / len(split))
        loudness = loudness * jnp.repeat(jnp.exp(draws), shape[dim] // parts).reshape((-1,) + (1,) * (len(shape) - 1 - dim))
    return loudness


def centred(rng, dims, deviation, bound, split=(), kind=jnp.bfloat16):
    result = deviation * jax.random.normal(rng, dims, jnp.float32)
    if split:
        result = result * level_of(rng, dims, split, -0.22, 0.18)
    return jnp.clip(result, -bound, bound).astype(kind)


def setup_inputs(seed: int = 0) -> dict:
    splits = jax.random.split(jax.random.key(seed), 5)
    stem_cache = centred(splits[0], (SLICES, 2, M, K), 1.0, 6.0, ((0, 256),))
    subtree_cache = centred(splits[1], (SLICES, 2, K, N), (2 * K) ** -0.5, 0.0625, ((0, 256),))
    final_gates = centred(splits[2], (2, N, N), (2 * N * SLICES) ** -0.5, 0.01171875)
    group_rows = with_ends(jax.random.randint(splits[3], (G,), 0, M // RB), jax.random.fold_in(splits[3], 1), 0, (M // RB) - 1).astype(jnp.int32)
    return dict(stem_cache=stem_cache, subtree_cache=subtree_cache, final_gates=final_gates, group_rows=group_rows)


def reference(stem_cache, subtree_cache, final_gates, group_rows):
    half = M // 2
    flip_a = (N_SA // 2) * N_SB * N_SL
    rows = jnp.arange(R, dtype=jnp.int32)
    source = (jnp.take(group_rows, rows // RB) * RB + rows % RB).astype(jnp.int32)

    def one_slice(index, total):
        lower = lax.dynamic_index_in_dim(stem_cache, index, 0, keepdims=False)
        other = lax.dynamic_index_in_dim(stem_cache, jnp.bitwise_xor(index, N_SL).astype(jnp.int32), 0, keepdims=False)
        stem = jnp.concatenate([lower[:, :half], other[:, half:]], axis=1)
        sub = lax.dynamic_index_in_dim(subtree_cache, jnp.bitwise_xor(index, flip_a).astype(jnp.int32), 0, keepdims=False)
        real = jnp.dot(stem[0], sub[0], preferred_element_type=jnp.float32) - jnp.dot(stem[1], sub[1], preferred_element_type=jnp.float32)
        imag = jnp.dot(stem[0], sub[1], preferred_element_type=jnp.float32) + jnp.dot(stem[1], sub[0], preferred_element_type=jnp.float32)
        partial_s = jnp.stack([real, imag]).astype(jnp.bfloat16)
        return total + jnp.take(partial_s, source, axis=1).astype(jnp.float32)

    summed = lax.fori_loop(0, SLICES, one_slice, jnp.zeros((2, R, N), jnp.float32))
    gates = final_gates.astype(jnp.float32)
    hp = lax.Precision.HIGHEST
    real = jnp.dot(summed[0], gates[0], precision=hp) - jnp.dot(summed[1], gates[1], precision=hp)
    imag = jnp.dot(summed[0], gates[1], precision=hp) + jnp.dot(summed[1], gates[0], precision=hp)
    return jnp.concatenate([real, imag], axis=1)
```

```python
import jax
import jax.numpy as jnp
from jax import lax
from jax.sharding import PartitionSpec as P

RB = 16
ALL = ("sa", "sb", "sl")


def swapped(shard, axis, apart):
    return lax.ppermute(shard, axis, [(i, i ^ 1 << apart) for i in range(lax.axis_size(axis))])


def complex_dot(left_real, left_imag, right, precision=None):
    dot = lambda a, b: jnp.dot(a, b, preferred_element_type=jnp.float32, precision=precision)
    real = dot(left_real, right[0]) - dot(left_imag, right[1])
    imag = dot(left_real, right[1]) + dot(left_imag, right[0])
    return (real, imag)


def local(stem_cache, subtree_cache, final_gates, group_rows):
    stem = stem_cache[0]
    half = stem.shape[1] // 2
    upper = swapped(stem[:, half:], "sb", 0)
    whole = jnp.concatenate([stem[:, :half], upper], axis=1)
    top_bit = lax.axis_size("sa").bit_length() - 2
    subtree = subtree_cache[0]
    left = swapped(whole, "sa", top_bit)
    real, imag = complex_dot(left[0], left[1], subtree)
    partial_s = jnp.stack([real, imag]).astype(jnp.bfloat16).astype(jnp.float32)
    summed = lax.psum(partial_s, ALL)
    total_rows = group_rows.shape[0] * RB
    own_count = total_rows // lax.axis_size(ALL)
    rows = lax.axis_index(ALL) * own_count + jnp.arange(own_count, dtype=jnp.int32)
    chosen = jnp.take(summed, jnp.take(group_rows, rows // RB) * RB + rows % RB, axis=1)
    gates = final_gates.astype(jnp.float32)
    out_real, out_imag = complex_dot(chosen[0], chosen[1], gates, precision=lax.Precision.HIGHEST)
    return jnp.concatenate([out_real, out_imag], axis=1)


def solution(mesh):
    return jax.shard_map(
        local,
        mesh=mesh,
        in_specs=(
            P(ALL, None, None, None),
            P(ALL, None, None, None),
            P(),
            P(),
        ),
        out_specs=P(ALL, None),
        check_vma=False,
    )
```

```python
import jax
import jax.numpy as jnp
from jax import lax
from jax.sharding import PartitionSpec as P

RB = 16
ALL = ("sa", "sb", "sl")


def swapped(shard, axis, apart):
    return lax.ppermute(shard, axis, [(i, i ^ 1 << apart) for i in range(lax.axis_size(axis))])


def complex_dot(left_real, left_imag, right, precision=None):
    dot = lambda a, b: jnp.dot(a, b, preferred_element_type=jnp.float32, precision=precision)
    real = dot(left_real, right[0]) - dot(left_imag, right[1])
    imag = dot(left_real, right[1]) + dot(left_imag, right[0])
    return (real, imag)


def halving(x, axis, dim):
    me = lax.axis_index(axis)
    for bit in reversed(range(lax.axis_size(axis).bit_length() - 1)):
        half = x.shape[dim] // 2
        lo = lax.slice_in_dim(x, 0, half, axis=dim)
        hi = lax.slice_in_dim(x, half, 2 * half, axis=dim)
        mine = (me >> bit) & 1
        keep = jnp.where(mine == 1, hi, lo)
        send = jnp.where(mine == 1, lo, hi)
        x = keep + swapped(send, axis, bit)
    return x


def doubling(x, axis):
    for bit in range(lax.axis_size(axis).bit_length() - 1):
        x = x + swapped(x, axis, bit)
    return x


def local(stem_cache, subtree_cache, final_gates, group_rows):
    stem = stem_cache[0]
    half = stem.shape[1] // 2
    upper = swapped(stem[:, half:], "sb", 0)
    whole = jnp.concatenate([stem[:, :half], upper], axis=1)
    top_bit = lax.axis_size("sa").bit_length() - 2
    subtree = subtree_cache[0]
    left = swapped(whole, "sa", top_bit)
    real, imag = complex_dot(left[0], left[1], subtree)
    partial_s = jnp.stack([real, imag]).astype(jnp.bfloat16).astype(jnp.float32)
    n_sl = lax.axis_size("sl")
    blocks = partial_s.shape[1] // RB
    own_count = RB // n_sl
    q = partial_s.reshape(2, blocks, n_sl, own_count, partial_s.shape[2])
    q = halving(q, "sl", 2)
    q = doubling(q, "sb")
    q = doubling(q, "sa")
    group = lax.axis_index("sa") * lax.axis_size("sb") + lax.axis_index("sb")
    chosen = jnp.take(q[:, :, 0], group_rows[group], axis=1)
    gates = final_gates.astype(jnp.float32)
    out_real, out_imag = complex_dot(chosen[0], chosen[1], gates, precision=lax.Precision.HIGHEST)
    return jnp.concatenate([out_real, out_imag], axis=1)


def solution(mesh):
    return jax.shard_map(
        local,
        mesh=mesh,
        in_specs=(
            P(ALL, None, None, None),
            P(ALL, None, None, None),
            P(),
            P(),
        ),
        out_specs=P(ALL, None),
        check_vma=False,
    )
```

```python
import jax
import jax.numpy as jnp
from jax import lax
from jax.sharding import PartitionSpec as P

RB = 16
ALL = ("sa", "sb", "sl")


def swapped(shard, axis, apart):
    return lax.ppermute(shard, axis, [(i, i ^ 1 << apart) for i in range(lax.axis_size(axis))])


def complex_dot(left_real, left_imag, right, precision=None):
    dot = lambda a, b: jnp.dot(a, b, preferred_element_type=jnp.float32, precision=precision)
    real = dot(left_real, right[0]) - dot(left_imag, right[1])
    imag = dot(left_real, right[1]) + dot(left_imag, right[0])
    return (real, imag)


def halving(x, axis, dim):
    me = lax.axis_index(axis)
    for bit in reversed(range(lax.axis_size(axis).bit_length() - 1)):
        half = x.shape[dim] // 2
        lo = lax.slice_in_dim(x, 0, half, axis=dim)
        hi = lax.slice_in_dim(x, half, 2 * half, axis=dim)
        mine = (me >> bit) & 1
        keep = jnp.where(mine == 1, hi, lo)
        send = jnp.where(mine == 1, lo, hi)
        x = keep + swapped(send, axis, bit)
    return x


def doubling(x, axis):
    for bit in range(lax.axis_size(axis).bit_length() - 1):
        x = x + swapped(x, axis, bit)
    return x


def local(stem_cache, subtree_cache, final_gates, group_rows):
    stem = stem_cache[0]
    half = stem.shape[1] // 2
    upper = swapped(stem[:, half:], "sb", 0)
    whole = jnp.concatenate([stem[:, :half], upper], axis=1)
    top_bit = lax.axis_size("sa").bit_length() - 2
    subtree = subtree_cache[0]
    left = swapped(whole, "sa", top_bit)
    real, imag = complex_dot(left[0], left[1], subtree)
    partial_s = jnp.stack([real, imag]).astype(jnp.bfloat16).astype(jnp.float32)
    n_sl = lax.axis_size("sl")
    blocks = partial_s.shape[1] // RB
    own_count = RB // n_sl
    q = partial_s.reshape(2, blocks, n_sl, own_count, partial_s.shape[2])
    q = lax.all_to_all(q, "sl", 2, 2, tiled=True).sum(axis=2)
    wanted = jnp.take(q, group_rows, axis=1)
    chosen = lax.all_to_all(wanted, ("sa", "sb"), 1, 1, tiled=True).sum(axis=1)
    gates = final_gates.astype(jnp.float32)
    out_real, out_imag = complex_dot(chosen[0], chosen[1], gates, precision=lax.Precision.HIGHEST)
    return jnp.concatenate([out_real, out_imag], axis=1)


def solution(mesh):
    return jax.shard_map(
        local,
        mesh=mesh,
        in_specs=(
            P(ALL, None, None, None),
            P(ALL, None, None, None),
            P(),
            P(),
        ),
        out_specs=P(ALL, None),
        check_vma=False,
    )
```

```python
import jax
import jax.numpy as jnp
from jax import lax
from jax.sharding import PartitionSpec as P

RB = 16
ALL = ("sa", "sb", "sl")


def complex_dot(left_real, left_imag, right, precision=None):
    dot = lambda a, b: jnp.dot(a, b, preferred_element_type=jnp.float32, precision=precision)
    real = dot(left_real, right[0]) - dot(left_imag, right[1])
    imag = dot(left_real, right[1]) + dot(left_imag, right[0])
    return (real, imag)


def stacked_dot(stem, subtree):
    rows = stem.shape[1]
    left = jnp.concatenate(
        [jnp.concatenate([stem[0], -stem[1]], axis=1), jnp.concatenate([stem[1], stem[0]], axis=1)], axis=0
    )
    right = subtree.reshape(-1, subtree.shape[-1])
    out = jnp.dot(left, right, preferred_element_type=jnp.float32)
    return out.reshape(2, rows, out.shape[-1])


def pair_sums(partial_s, n_sl):
    blocks = partial_s.shape[1] // RB
    q = partial_s.astype(jnp.bfloat16).astype(jnp.float32)
    q = q.reshape(2, blocks, n_sl, RB // n_sl, partial_s.shape[2])
    return lax.all_to_all(q, "sl", 2, 2, tiled=True).sum(axis=2)


def local(stem_cache, subtree_cache, final_gates, group_rows):
    stem = stem_cache[0]
    subtree = subtree_cache[0]
    half = stem.shape[1] // 2
    n_sa, n_sb, n_sl = lax.axis_size("sa"), lax.axis_size("sb"), lax.axis_size("sl")
    flip = n_sa // 2
    lower = lax.ppermute(stem[:, :half], "sa", [(i, i ^ flip) for i in range(n_sa)])
    upper_src, _ = lax.optimization_barrier((stem[:, half:], lower))
    upper = lax.ppermute(
        upper_src,
        ("sa", "sb"),
        [(a * n_sb + b, (a ^ flip) * n_sb + (b ^ 1)) for a in range(n_sa) for b in range(n_sb)],
    )
    q_lower = pair_sums(stacked_dot(lower, subtree), n_sl)
    q_upper = pair_sums(stacked_dot(upper, subtree), n_sl)
    q = jnp.concatenate([q_lower, q_upper], axis=1)
    wanted = jnp.take(q, group_rows, axis=1)
    chosen = lax.all_to_all(wanted, ("sa", "sb"), 1, 1, tiled=True).sum(axis=1)
    gates = final_gates.astype(jnp.float32)
    out_real, out_imag = complex_dot(chosen[0], chosen[1], gates, precision=lax.Precision.HIGHEST)
    return jnp.concatenate([out_real, out_imag], axis=1)


def solution(mesh):
    return jax.shard_map(
        local,
        mesh=mesh,
        in_specs=(
            P(ALL, None, None, None),
            P(ALL, None, None, None),
            P(),
            P(),
        ),
        out_specs=P(ALL, None),
        check_vma=False,
    )
```

```python
import jax
import jax.numpy as jnp
from jax import lax
from jax.sharding import PartitionSpec as P

RB = 16
ALL = ("sa", "sb", "sl")


def complex_dot(left_real, left_imag, right, precision=None):
    dot = lambda a, b: jnp.dot(a, b, preferred_element_type=jnp.float32, precision=precision)
    real = dot(left_real, right[0]) - dot(left_imag, right[1])
    imag = dot(left_real, right[1]) + dot(left_imag, right[0])
    return (real, imag)


def stacked_dot(stem, subtree):
    rows = stem.shape[1]
    left = jnp.concatenate(
        [jnp.concatenate([stem[0], -stem[1]], axis=1), jnp.concatenate([stem[1], stem[0]], axis=1)], axis=0
    )
    right = subtree.reshape(-1, subtree.shape[-1])
    out = jnp.dot(left, right, preferred_element_type=jnp.float32)
    return out.reshape(2, rows, out.shape[-1])


def pair_sums(partial_s, n_sl):
    blocks = partial_s.shape[1] // RB
    q = lax.reduce_precision(partial_s, exponent_bits=8, mantissa_bits=7)
    q = q.reshape(2, blocks, n_sl, RB // n_sl, partial_s.shape[2])
    return lax.all_to_all(q, "sl", 2, 2, tiled=True).sum(axis=2)


def local(stem_cache, subtree_cache, final_gates, group_rows):
    stem = stem_cache[0]
    subtree = subtree_cache[0]
    half = stem.shape[1] // 2
    n_sa, n_sb, n_sl = lax.axis_size("sa"), lax.axis_size("sb"), lax.axis_size("sl")
    flip = n_sa // 2
    lower = lax.ppermute(stem[:, :half], "sa", [(i, i ^ flip) for i in range(n_sa)])
    upper_src, _ = lax.optimization_barrier((stem[:, half:], lower))
    upper = lax.ppermute(
        upper_src,
        ("sa", "sb"),
        [(a * n_sb + b, (a ^ flip) * n_sb + (b ^ 1)) for a in range(n_sa) for b in range(n_sb)],
    )
    q_lower = pair_sums(stacked_dot(lower, subtree), n_sl)
    q_upper = pair_sums(stacked_dot(upper, subtree), n_sl)
    q = jnp.concatenate([q_lower, q_upper], axis=1)
    wanted = jnp.take(q, group_rows, axis=1)
    chosen = lax.all_to_all(wanted, ("sa", "sb"), 1, 1, tiled=True).sum(axis=1)
    gates = final_gates.astype(jnp.float32)
    out_real, out_imag = complex_dot(chosen[0], chosen[1], gates, precision=lax.Precision.HIGHEST)
    return jnp.concatenate([out_real, out_imag], axis=1)


def solution(mesh):
    return jax.shard_map(
        local,
        mesh=mesh,
        in_specs=(
            P(ALL, None, None, None),
            P(ALL, None, None, None),
            P(),
            P(),
        ),
        out_specs=P(ALL, None),
        check_vma=False,
    )
```

```python
import jax
import jax.numpy as jnp
from jax import lax
from jax.sharding import PartitionSpec as P

RB = 16
ALL = ("sa", "sb", "sl")


def complex_dot(left_real, left_imag, right, precision=None):
    dot = lambda a, b: jnp.dot(a, b, preferred_element_type=jnp.float32, precision=precision)
    real = dot(left_real, right[0]) - dot(left_imag, right[1])
    imag = dot(left_real, right[1]) + dot(left_imag, right[0])
    return (real, imag)


def stacked_dot(stem, subtree):
    rows = stem.shape[1]
    left = jnp.concatenate(
        [jnp.concatenate([stem[0], -stem[1]], axis=1), jnp.concatenate([stem[1], stem[0]], axis=1)], axis=0
    )
    right = subtree.reshape(-1, subtree.shape[-1])
    out = jnp.dot(left, right, preferred_element_type=jnp.float32)
    return out.reshape(2, rows, out.shape[-1])


def pair_sums(partial_s, n_sl):
    blocks = partial_s.shape[1] // RB
    q = lax.reduce_precision(partial_s, exponent_bits=8, mantissa_bits=7)
    q = q.reshape(2, blocks, n_sl, RB // n_sl, partial_s.shape[2])
    return lax.all_to_all(q, "sl", 2, 2, tiled=True).sum(axis=2)


def local(stem_cache, subtree_cache, final_gates, group_rows):
    stem = stem_cache[0]
    subtree = subtree_cache[0]
    rows = stem.shape[1]
    half = rows // 2
    n_sa, n_sb, n_sl = lax.axis_size("sa"), lax.axis_size("sb"), lax.axis_size("sl")
    flip = n_sa // 2
    straight = [(i, i ^ flip) for i in range(n_sa)]
    diagonal = [(a * n_sb + b, (a ^ flip) * n_sb + (b ^ 1)) for a in range(n_sa) for b in range(n_sb)]
    cut = rows - rows // 4
    lower = lax.ppermute(stem[:, :half], "sa", straight)
    middle = lax.ppermute(stem[:, half:cut], ("sa", "sb"), diagonal)
    last_src, _, _ = lax.optimization_barrier((stem[:, cut:], lower, middle))
    last = lax.ppermute(last_src, ("sa", "sb"), diagonal)
    first = jnp.concatenate([lower, middle], axis=1)
    q_first = pair_sums(stacked_dot(first, subtree), n_sl)
    q_last = pair_sums(stacked_dot(last, subtree), n_sl)
    q = jnp.concatenate([q_first, q_last], axis=1)
    wanted = jnp.take(q, group_rows, axis=1)
    chosen = lax.all_to_all(wanted, ("sa", "sb"), 1, 1, tiled=True).sum(axis=1)
    gates = final_gates.astype(jnp.float32)
    out_real, out_imag = complex_dot(chosen[0], chosen[1], gates, precision=lax.Precision.HIGHEST)
    return jnp.concatenate([out_real, out_imag], axis=1)


def solution(mesh):
    return jax.shard_map(
        local,
        mesh=mesh,
        in_specs=(
            P(ALL, None, None, None),
            P(ALL, None, None, None),
            P(),
            P(),
        ),
        out_specs=P(ALL, None),
        check_vma=False,
    )
```

```python
import jax
import jax.numpy as jnp
from jax import lax
from jax.sharding import PartitionSpec as P

RB = 16
ALL = ("sa", "sb", "sl")


def complex_dot(left_real, left_imag, right, precision=None):
    dot = lambda a, b: jnp.dot(a, b, preferred_element_type=jnp.float32, precision=precision)
    real = dot(left_real, right[0]) - dot(left_imag, right[1])
    imag = dot(left_real, right[1]) + dot(left_imag, right[0])
    return (real, imag)


def stacked_dot(stem, subtree):
    rows = stem.shape[1]
    left = jnp.concatenate(
        [jnp.concatenate([stem[0], -stem[1]], axis=1), jnp.concatenate([stem[1], stem[0]], axis=1)], axis=0
    )
    right = subtree.reshape(-1, subtree.shape[-1])
    out = jnp.dot(left, right, preferred_element_type=jnp.float32)
    return out.reshape(2, rows, out.shape[-1])


def pair_sums(partial_s, n_sl):
    blocks = partial_s.shape[1] // RB
    q = lax.reduce_precision(partial_s, exponent_bits=8, mantissa_bits=7)
    q = q.reshape(2, blocks, n_sl, RB // n_sl, partial_s.shape[2])
    return lax.all_to_all(q, "sl", 2, 2, tiled=True).sum(axis=2)


def local(stem_cache, subtree_cache, final_gates, group_rows):
    stem = stem_cache[0]
    subtree = subtree_cache[0]
    rows = stem.shape[1]
    half = rows // 2
    n_sa, n_sb, n_sl = lax.axis_size("sa"), lax.axis_size("sb"), lax.axis_size("sl")
    flip = n_sa // 2
    straight = [(i, i ^ flip) for i in range(n_sa)]
    diagonal = [(a * n_sb + b, (a ^ flip) * n_sb + (b ^ 1)) for a in range(n_sa) for b in range(n_sb)]
    cut = rows - rows // 4
    lower = lax.ppermute(stem[:, :half], "sa", straight)
    middle = lax.ppermute(stem[:, half:cut], ("sa", "sb"), diagonal)
    last_src, _, _ = lax.optimization_barrier((stem[:, cut:], lower, middle))
    last = lax.ppermute(last_src, ("sa", "sb"), diagonal)
    partial_s = jnp.concatenate(
        [stacked_dot(lower, subtree), stacked_dot(middle, subtree), stacked_dot(last, subtree)], axis=1
    )
    q = pair_sums(partial_s, n_sl)
    wanted = jnp.take(q, group_rows, axis=1)
    chosen = lax.all_to_all(wanted, ("sa", "sb"), 1, 1, tiled=True).sum(axis=1)
    gates = final_gates.astype(jnp.float32)
    out_real, out_imag = complex_dot(chosen[0], chosen[1], gates, precision=lax.Precision.HIGHEST)
    return jnp.concatenate([out_real, out_imag], axis=1)


def solution(mesh):
    return jax.shard_map(
        local,
        mesh=mesh,
        in_specs=(
            P(ALL, None, None, None),
            P(ALL, None, None, None),
            P(),
            P(),
        ),
        out_specs=P(ALL, None),
        check_vma=False,
    )
```

```python
import jax
import jax.numpy as jnp
from jax import lax
from jax.sharding import PartitionSpec as P

RB = 16
ALL = ("sa", "sb", "sl")


def complex_dot(left_real, left_imag, right, precision=None):
    dot = lambda a, b: jnp.dot(a, b, preferred_element_type=jnp.float32, precision=precision)
    real = dot(left_real, right[0]) - dot(left_imag, right[1])
    imag = dot(left_real, right[1]) + dot(left_imag, right[0])
    return (real, imag)


def stacked_dot(stem, subtree):
    rows = stem.shape[1]
    left = jnp.concatenate(
        [jnp.concatenate([stem[0], -stem[1]], axis=1), jnp.concatenate([stem[1], stem[0]], axis=1)], axis=0
    )
    right = subtree.reshape(-1, subtree.shape[-1])
    out = jnp.dot(left, right, preferred_element_type=jnp.float32)
    return out.reshape(2, rows, out.shape[-1])


def pair_sums(partial_s, n_sl):
    blocks = partial_s.shape[1] // RB
    q = lax.reduce_precision(partial_s, exponent_bits=8, mantissa_bits=7)
    q = q.reshape(2, blocks, n_sl, RB // n_sl, partial_s.shape[2])
    return lax.all_to_all(q, "sl", 2, 2, tiled=True).sum(axis=2)


def local(stem_cache, subtree_cache, final_gates, group_rows):
    stem = stem_cache[0]
    subtree = subtree_cache[0]
    rows = stem.shape[1]
    half = rows // 2
    n_sa, n_sb, n_sl = lax.axis_size("sa"), lax.axis_size("sb"), lax.axis_size("sl")
    flip = n_sa // 2
    straight = [(i, i ^ flip) for i in range(n_sa)]
    diagonal = [(a * n_sb + b, (a ^ flip) * n_sb + (b ^ 1)) for a in range(n_sa) for b in range(n_sb)]
    cut = rows - rows // 4
    lower = lax.ppermute(stem[:, :half], "sa", straight)
    middle = lax.ppermute(stem[:, half:cut], ("sa", "sb"), diagonal)
    last_src, _, _ = lax.optimization_barrier((stem[:, cut:], lower, middle))
    last = lax.ppermute(last_src, ("sa", "sb"), diagonal)
    first = jnp.concatenate([stacked_dot(lower, subtree), stacked_dot(middle, subtree)], axis=1)
    q_first = pair_sums(first, n_sl)
    q_last = pair_sums(stacked_dot(last, subtree), n_sl)
    q = jnp.concatenate([q_first, q_last], axis=1)
    wanted = jnp.take(q, group_rows, axis=1)
    chosen = lax.all_to_all(wanted, ("sa", "sb"), 1, 1, tiled=True).sum(axis=1)
    gates = final_gates.astype(jnp.float32)
    out_real, out_imag = complex_dot(chosen[0], chosen[1], gates, precision=lax.Precision.HIGHEST)
    return jnp.concatenate([out_real, out_imag], axis=1)


def solution(mesh):
    return jax.shard_map(
        local,
        mesh=mesh,
        in_specs=(
            P(ALL, None, None, None),
            P(ALL, None, None, None),
            P(),
            P(),
        ),
        out_specs=P(ALL, None),
        check_vma=False,
    )
```

```python
import jax
import jax.numpy as jnp
from jax import lax
from jax.sharding import PartitionSpec as P

RB = 16
ALL = ("sa", "sb", "sl")


def complex_dot(left_real, left_imag, right, precision=None):
    dot = lambda a, b: jnp.dot(a, b, preferred_element_type=jnp.float32, precision=precision)
    real = dot(left_real, right[0]) - dot(left_imag, right[1])
    imag = dot(left_real, right[1]) + dot(left_imag, right[0])
    return (real, imag)


def stacked_dot(stem, subtree):
    rows = stem.shape[1]
    left = jnp.concatenate(
        [jnp.concatenate([stem[0], -stem[1]], axis=1), jnp.concatenate([stem[1], stem[0]], axis=1)], axis=0
    )
    right = subtree.reshape(-1, subtree.shape[-1])
    out = jnp.dot(left, right, preferred_element_type=jnp.float32)
    return out.reshape(2, rows, out.shape[-1])


def pair_sums(partial_s, n_sl):
    blocks = partial_s.shape[1] // RB
    q = lax.reduce_precision(partial_s, exponent_bits=8, mantissa_bits=7)
    q = q.reshape(2, blocks, n_sl, RB // n_sl, partial_s.shape[2])
    return lax.all_to_all(q, "sl", 2, 2, tiled=True).sum(axis=2)


def local(stem_cache, subtree_cache, final_gates, group_rows):
    stem = stem_cache[0]
    subtree = subtree_cache[0]
    rows = stem.shape[1]
    half = rows // 2
    n_sa, n_sb, n_sl = lax.axis_size("sa"), lax.axis_size("sb"), lax.axis_size("sl")
    flip = n_sa // 2
    straight = [(i, i ^ flip) for i in range(n_sa)]
    diagonal = [(a * n_sb + b, (a ^ flip) * n_sb + (b ^ 1)) for a in range(n_sa) for b in range(n_sb)]
    cut = rows - RB
    lower = lax.ppermute(stem[:, :half], "sa", straight)
    middle = lax.ppermute(stem[:, half:cut], ("sa", "sb"), diagonal)
    last_src, _, _ = lax.optimization_barrier((stem[:, cut:], lower, middle))
    last = lax.ppermute(last_src, ("sa", "sb"), diagonal)
    first = jnp.concatenate([stacked_dot(lower, subtree), stacked_dot(middle, subtree)], axis=1)
    q_first = pair_sums(first, n_sl)
    last, q_first = lax.optimization_barrier((last, q_first))
    q_last = pair_sums(stacked_dot(last, subtree), n_sl)
    q = jnp.concatenate([q_first, q_last], axis=1)
    wanted = jnp.take(q, group_rows, axis=1)
    chosen = lax.all_to_all(wanted, ("sa", "sb"), 1, 1, tiled=True).sum(axis=1)
    gates = final_gates.astype(jnp.float32)
    out_real, out_imag = complex_dot(chosen[0], chosen[1], gates, precision=lax.Precision.HIGHEST)
    return jnp.concatenate([out_real, out_imag], axis=1)


def solution(mesh):
    return jax.shard_map(
        local,
        mesh=mesh,
        in_specs=(
            P(ALL, None, None, None),
            P(ALL, None, None, None),
            P(),
            P(),
        ),
        out_specs=P(ALL, None),
        check_vma=False,
    )
```

```python
import jax
import jax.numpy as jnp
from jax import lax
from jax.sharding import PartitionSpec as P

RB = 16
ALL = ("sa", "sb", "sl")


def complex_dot(left_real, left_imag, right, precision=None):
    dot = lambda a, b: jnp.dot(a, b, preferred_element_type=jnp.float32, precision=precision)
    real = dot(left_real, right[0]) - dot(left_imag, right[1])
    imag = dot(left_real, right[1]) + dot(left_imag, right[0])
    return (real, imag)


def stacked_dot(stem, subtree):
    rows = stem.shape[1]
    left = jnp.concatenate(
        [jnp.concatenate([stem[0], -stem[1]], axis=1), jnp.concatenate([stem[1], stem[0]], axis=1)], axis=0
    )
    right = subtree.reshape(-1, subtree.shape[-1])
    out = jnp.dot(left, right, preferred_element_type=jnp.float32)
    return out.reshape(2, rows, out.shape[-1])


def pair_sums(partial_s, n_sl):
    blocks = partial_s.shape[1] // RB
    q = lax.reduce_precision(partial_s, exponent_bits=8, mantissa_bits=7)
    q = q.reshape(2, blocks, n_sl, RB // n_sl, partial_s.shape[2])
    return lax.all_to_all(q, "sl", 2, 2, tiled=True).sum(axis=2)


def local(stem_cache, subtree_cache, final_gates, group_rows):
    stem = stem_cache[0]
    subtree = subtree_cache[0]
    rows = stem.shape[1]
    half = rows // 2
    n_sa, n_sb, n_sl = lax.axis_size("sa"), lax.axis_size("sb"), lax.axis_size("sl")
    flip = n_sa // 2
    straight = [(i, i ^ flip) for i in range(n_sa)]
    diagonal = [(a * n_sb + b, (a ^ flip) * n_sb + (b ^ 1)) for a in range(n_sa) for b in range(n_sb)]
    cut = rows - rows // 4
    lower = lax.ppermute(stem[:, :half], "sa", straight)
    middle = lax.ppermute(stem[:, half:cut], ("sa", "sb"), diagonal)
    end_src, _ = lax.optimization_barrier((stem[:, cut:], middle))
    end = lax.ppermute(end_src, ("sa", "sb"), diagonal)
    q_middle = pair_sums(stacked_dot(middle, subtree), n_sl)
    lower, end, q_middle = lax.optimization_barrier((lower, end, q_middle))
    q_rest = pair_sums(jnp.concatenate([stacked_dot(lower, subtree), stacked_dot(end, subtree)], axis=1), n_sl)
    blocks_lower = half // RB
    q = jnp.concatenate([q_rest[:, :blocks_lower], q_middle, q_rest[:, blocks_lower:]], axis=1)
    wanted = jnp.take(q, group_rows, axis=1)
    chosen = lax.all_to_all(wanted, ("sa", "sb"), 1, 1, tiled=True).sum(axis=1)
    gates = final_gates.astype(jnp.float32)
    out_real, out_imag = complex_dot(chosen[0], chosen[1], gates, precision=lax.Precision.HIGHEST)
    return jnp.concatenate([out_real, out_imag], axis=1)


def solution(mesh):
    return jax.shard_map(
        local,
        mesh=mesh,
        in_specs=(
            P(ALL, None, None, None),
            P(ALL, None, None, None),
            P(),
            P(),
        ),
        out_specs=P(ALL, None),
        check_vma=False,
    )
```

```python
import jax
import jax.numpy as jnp
from jax import lax
from jax.sharding import PartitionSpec as P

RB = 16
ALL = ("sa", "sb", "sl")


def complex_dot(left_real, left_imag, right, precision=None):
    dot = lambda a, b: jnp.dot(a, b, preferred_element_type=jnp.float32, precision=precision)
    real = dot(left_real, right[0]) - dot(left_imag, right[1])
    imag = dot(left_real, right[1]) + dot(left_imag, right[0])
    return (real, imag)


def stacked_dot(stem, subtree):
    rows = stem.shape[1]
    left = jnp.concatenate(
        [jnp.concatenate([stem[0], -stem[1]], axis=1), jnp.concatenate([stem[1], stem[0]], axis=1)], axis=0
    )
    right = subtree.reshape(-1, subtree.shape[-1])
    out = jnp.dot(left, right, preferred_element_type=jnp.float32)
    return out.reshape(2, rows, out.shape[-1])


def pair_sums(partial_s, n_sl):
    blocks = partial_s.shape[1] // RB
    q = lax.reduce_precision(partial_s, exponent_bits=8, mantissa_bits=7)
    q = q.reshape(2, blocks, n_sl, RB // n_sl, partial_s.shape[2])
    return lax.all_to_all(q, "sl", 2, 2, tiled=True).sum(axis=2)


def local(stem_cache, subtree_cache, final_gates, group_rows):
    stem = stem_cache[0]
    subtree = subtree_cache[0]
    rows = stem.shape[1]
    half = rows // 2
    n_sa, n_sb, n_sl = lax.axis_size("sa"), lax.axis_size("sb"), lax.axis_size("sl")
    flip = n_sa // 2
    straight = [(i, i ^ flip) for i in range(n_sa)]
    diagonal = [(a * n_sb + b, (a ^ flip) * n_sb + (b ^ 1)) for a in range(n_sa) for b in range(n_sb)]
    cut = rows - rows // 4
    lower = lax.ppermute(stem[:, :half], "sa", straight)
    middle = lax.ppermute(stem[:, half:cut], ("sa", "sb"), diagonal)
    end_src, _ = lax.optimization_barrier((stem[:, cut:], middle))
    end = lax.ppermute(end_src, ("sa", "sb"), diagonal)
    q_middle = pair_sums(stacked_dot(middle, subtree), n_sl)
    q_lower = pair_sums(stacked_dot(lower, subtree), n_sl)
    end, q_lower = lax.optimization_barrier((end, q_lower))
    q_end = pair_sums(stacked_dot(end, subtree), n_sl)
    q = jnp.concatenate([q_lower, q_middle, q_end], axis=1)
    wanted = jnp.take(q, group_rows, axis=1)
    chosen = lax.all_to_all(wanted, ("sa", "sb"), 1, 1, tiled=True).sum(axis=1)
    gates = final_gates.astype(jnp.float32)
    out_real, out_imag = complex_dot(chosen[0], chosen[1], gates, precision=lax.Precision.HIGHEST)
    return jnp.concatenate([out_real, out_imag], axis=1)


def solution(mesh):
    return jax.shard_map(
        local,
        mesh=mesh,
        in_specs=(
            P(ALL, None, None, None),
            P(ALL, None, None, None),
            P(),
            P(),
        ),
        out_specs=P(ALL, None),
        check_vma=False,
    )
```

```python
import jax
import jax.numpy as jnp
from jax import lax
from jax.sharding import PartitionSpec as P
from jax.experimental import pallas as pl

RB = 16
ALL = ("sa", "sb", "sl")


def complex_dot(left_real, left_imag, right, precision=None):
    dot = lambda a, b: jnp.dot(a, b, preferred_element_type=jnp.float32, precision=precision)
    real = dot(left_real, right[0]) - dot(left_imag, right[1])
    imag = dot(left_real, right[1]) + dot(left_imag, right[0])
    return (real, imag)


def _acc_kernel(left_ref, right_ref, out_ref):
    @pl.when(pl.program_id(0) == 0)
    def _():
        out_ref[...] = jnp.zeros_like(out_ref)

    out_ref[...] += jnp.dot(left_ref[...], right_ref[...], preferred_element_type=jnp.float32)


def streamed_dot(left, right, block_k=1024):
    m, k = left.shape
    n = right.shape[1]
    return pl.pallas_call(
        _acc_kernel,
        grid=(k // block_k,),
        in_specs=[
            pl.BlockSpec((m, block_k), lambda i: (0, i)),
            pl.BlockSpec((block_k, n), lambda i: (i, 0)),
        ],
        out_specs=pl.BlockSpec((m, n), lambda i: (0, 0)),
        out_shape=jax.ShapeDtypeStruct((m, n), jnp.float32),
    )(left, right)


def stacked_dot(stem, subtree, dot=None):
    rows = stem.shape[1]
    left = jnp.concatenate(
        [jnp.concatenate([stem[0], -stem[1]], axis=1), jnp.concatenate([stem[1], stem[0]], axis=1)], axis=0
    )
    right = subtree.reshape(-1, subtree.shape[-1])
    if dot is None:
        out = jnp.dot(left, right, preferred_element_type=jnp.float32)
    else:
        out = dot(left, right)
    return out.reshape(2, rows, out.shape[-1])


def pair_sums(partial_s, n_sl):
    blocks = partial_s.shape[1] // RB
    q = lax.reduce_precision(partial_s, exponent_bits=8, mantissa_bits=7)
    q = q.reshape(2, blocks, n_sl, RB // n_sl, partial_s.shape[2])
    return lax.all_to_all(q, "sl", 2, 2, tiled=True).sum(axis=2)


def local(stem_cache, subtree_cache, final_gates, group_rows):
    stem = stem_cache[0]
    subtree = subtree_cache[0]
    rows = stem.shape[1]
    half = rows // 2
    n_sa, n_sb, n_sl = lax.axis_size("sa"), lax.axis_size("sb"), lax.axis_size("sl")
    flip = n_sa // 2
    straight = [(i, i ^ flip) for i in range(n_sa)]
    diagonal = [(a * n_sb + b, (a ^ flip) * n_sb + (b ^ 1)) for a in range(n_sa) for b in range(n_sb)]
    cut = rows - rows // 4
    lower = lax.ppermute(stem[:, :half], "sa", straight)
    middle = lax.ppermute(stem[:, half:cut], ("sa", "sb"), diagonal)
    last_src, _, _ = lax.optimization_barrier((stem[:, cut:], lower, middle))
    last = lax.ppermute(last_src, ("sa", "sb"), diagonal)
    first = jnp.concatenate([lower, middle], axis=1)
    q_first = pair_sums(stacked_dot(first, subtree), n_sl)
    q_last = pair_sums(stacked_dot(last, subtree, streamed_dot), n_sl)
    q = jnp.concatenate([q_first, q_last], axis=1)
    wanted = jnp.take(q, group_rows, axis=1)
    chosen = lax.all_to_all(wanted, ("sa", "sb"), 1, 1, tiled=True).sum(axis=1)
    gates = final_gates.astype(jnp.float32)
    out_real, out_imag = complex_dot(chosen[0], chosen[1], gates, precision=lax.Precision.HIGHEST)
    return jnp.concatenate([out_real, out_imag], axis=1)


def solution(mesh):
    return jax.shard_map(
        local,
        mesh=mesh,
        in_specs=(
            P(ALL, None, None, None),
            P(ALL, None, None, None),
            P(),
            P(),
        ),
        out_specs=P(ALL, None),
        check_vma=False,
    )
```

```python
import jax
import jax.numpy as jnp
from jax import lax
from jax.sharding import PartitionSpec as P

RB = 16
ALL = ("sa", "sb", "sl")


def complex_dot(left_real, left_imag, right, precision=None):
    dot = lambda a, b: jnp.dot(a, b, preferred_element_type=jnp.float32, precision=precision)
    real = dot(left_real, right[0]) - dot(left_imag, right[1])
    imag = dot(left_real, right[1]) + dot(left_imag, right[0])
    return (real, imag)


def stacked_dot(stem, subtree):
    rows = stem.shape[1]
    left = jnp.concatenate(
        [jnp.concatenate([stem[0], -stem[1]], axis=1), jnp.concatenate([stem[1], stem[0]], axis=1)], axis=0
    )
    right = subtree.reshape(-1, subtree.shape[-1])
    out = jnp.dot(left, right, preferred_element_type=jnp.float32)
    return out.reshape(2, rows, out.shape[-1])


def pair_sums(partial_s, n_sl):
    blocks = partial_s.shape[1] // RB
    q = lax.reduce_precision(partial_s, exponent_bits=8, mantissa_bits=7)
    q = q.reshape(2, blocks, n_sl, RB // n_sl, partial_s.shape[2])
    return lax.all_to_all(q, "sl", 2, 2, tiled=True).sum(axis=2)


def local(stem_cache, subtree_cache, final_gates, group_rows):
    stem = stem_cache[0]
    subtree = subtree_cache[0]
    rows = stem.shape[1]
    half = rows // 2
    n_sa, n_sb, n_sl = lax.axis_size("sa"), lax.axis_size("sb"), lax.axis_size("sl")
    flip = n_sa // 2
    straight = [(i, i ^ flip) for i in range(n_sa)]
    diagonal = [(a * n_sb + b, (a ^ flip) * n_sb + (b ^ 1)) for a in range(n_sa) for b in range(n_sb)]
    cut = rows - rows // 4
    lower = lax.ppermute(stem[:, :half], "sa", straight)
    middle = lax.ppermute(stem[:, half:cut], ("sa", "sb"), diagonal)
    last_src, _, _ = lax.optimization_barrier((stem[:, cut:], lower, middle))
    last = lax.ppermute(last_src, ("sa", "sb"), diagonal)
    first = jnp.concatenate([lower, middle], axis=1)
    q_first = pair_sums(stacked_dot(first, subtree), n_sl)
    q_last = pair_sums(stacked_dot(last, subtree), n_sl)
    q = jnp.concatenate([q_first, q_last], axis=1)
    wanted = jnp.take(q, group_rows, axis=1)
    chosen = lax.all_to_all(wanted, ("sa", "sb"), 1, 1, tiled=True).sum(axis=1)
    gates = final_gates.astype(jnp.float32)
    block = jnp.concatenate(
        [jnp.concatenate([gates[0], gates[1]], axis=1), jnp.concatenate([-gates[1], gates[0]], axis=1)], axis=0
    )
    left = jnp.concatenate([chosen[0], chosen[1]], axis=1)
    return jnp.dot(left, block, preferred_element_type=jnp.float32, precision=lax.Precision.HIGHEST)


def solution(mesh):
    return jax.shard_map(
        local,
        mesh=mesh,
        in_specs=(
            P(ALL, None, None, None),
            P(ALL, None, None, None),
            P(),
            P(),
        ),
        out_specs=P(ALL, None),
        check_vma=False,
    )
```

```python
import jax
import jax.numpy as jnp
from jax import lax
from jax.sharding import PartitionSpec as P

RB = 16
ALL = ("sa", "sb", "sl")


def complex_dot(left_real, left_imag, right, precision=None):
    dot = lambda a, b: jnp.dot(a, b, preferred_element_type=jnp.float32, precision=precision)
    real = dot(left_real, right[0]) - dot(left_imag, right[1])
    imag = dot(left_real, right[1]) + dot(left_imag, right[0])
    return (real, imag)


def stacked_dot(stem, subtree):
    rows = stem.shape[1]
    left = jnp.concatenate(
        [jnp.concatenate([stem[0], -stem[1]], axis=1), jnp.concatenate([stem[1], stem[0]], axis=1)], axis=0
    )
    right = subtree.reshape(-1, subtree.shape[-1])
    out = jnp.dot(left, right, preferred_element_type=jnp.float32)
    return out.reshape(2, rows, out.shape[-1])


def pair_sums(partial_s, n_sl):
    blocks = partial_s.shape[1] // RB
    q = lax.reduce_precision(partial_s, exponent_bits=8, mantissa_bits=7)
    q = q.reshape(2, blocks, n_sl, RB // n_sl, partial_s.shape[2])
    return lax.all_to_all(q, "sl", 2, 2, tiled=True).sum(axis=2)


def local(stem_cache, subtree_cache, final_gates, group_rows):
    stem = stem_cache[0]
    subtree = subtree_cache[0]
    rows = stem.shape[1]
    half = rows // 2
    n_sa, n_sb, n_sl = lax.axis_size("sa"), lax.axis_size("sb"), lax.axis_size("sl")
    flip = n_sa // 2
    straight = [(i, i ^ flip) for i in range(n_sa)]
    diagonal = [(a * n_sb + b, (a ^ flip) * n_sb + (b ^ 1)) for a in range(n_sa) for b in range(n_sb)]
    cut = rows - rows // 4
    lower_parts = [lax.ppermute(stem[part, :half], "sa", straight) for part in range(2)]
    middle_parts = [lax.ppermute(stem[part, half:cut], ("sa", "sb"), diagonal) for part in range(2)]
    last_src, *landed = lax.optimization_barrier((stem[:, cut:], *lower_parts, *middle_parts))
    lower, middle = jnp.stack(landed[:2]), jnp.stack(landed[2:])
    last = lax.ppermute(last_src, ("sa", "sb"), diagonal)
    first = jnp.concatenate([lower, middle], axis=1)
    q_first = pair_sums(stacked_dot(first, subtree), n_sl)
    q_last = pair_sums(stacked_dot(last, subtree), n_sl)
    q = jnp.concatenate([q_first, q_last], axis=1)
    wanted = jnp.take(q, group_rows, axis=1)
    chosen = lax.all_to_all(wanted, ("sa", "sb"), 1, 1, tiled=True).sum(axis=1)
    gates = final_gates.astype(jnp.float32)
    out_real, out_imag = complex_dot(chosen[0], chosen[1], gates, precision=lax.Precision.HIGHEST)
    return jnp.concatenate([out_real, out_imag], axis=1)


def solution(mesh):
    return jax.shard_map(
        local,
        mesh=mesh,
        in_specs=(
            P(ALL, None, None, None),
            P(ALL, None, None, None),
            P(),
            P(),
        ),
        out_specs=P(ALL, None),
        check_vma=False,
    )
```

```python
import jax
import jax.numpy as jnp
from jax import lax
from jax.sharding import PartitionSpec as P

RB = 16
ALL = ("sa", "sb", "sl")


def complex_dot(left_real, left_imag, right, precision=None):
    dot = lambda a, b: jnp.dot(a, b, preferred_element_type=jnp.float32, precision=precision)
    real = dot(left_real, right[0]) - dot(left_imag, right[1])
    imag = dot(left_real, right[1]) + dot(left_imag, right[0])
    return (real, imag)


def stacked_dot(stem, subtree):
    rows = stem.shape[1]
    left = jnp.concatenate(
        [jnp.concatenate([stem[0], -stem[1]], axis=1), jnp.concatenate([stem[1], stem[0]], axis=1)], axis=0
    )
    right = subtree.reshape(-1, subtree.shape[-1])
    out = jnp.dot(left, right, preferred_element_type=jnp.float32)
    return out.reshape(2, rows, out.shape[-1])


def pair_sums(partial_s, n_sl):
    blocks = partial_s.shape[1] // RB
    q = lax.reduce_precision(partial_s, exponent_bits=8, mantissa_bits=7)
    q = q.reshape(2, blocks, n_sl, RB // n_sl, partial_s.shape[2])
    return lax.all_to_all(q, "sl", 2, 2, tiled=True).sum(axis=2)


def pair_major_sums(stem, subtree, n_sl):
    blocks = stem.shape[1] // RB
    k = stem.shape[2]
    parts = stem.reshape(2, blocks, n_sl, RB // n_sl, k)
    left = jnp.stack(
        [jnp.concatenate([parts[0], -parts[1]], axis=-1), jnp.concatenate([parts[1], parts[0]], axis=-1)]
    )
    left = jnp.transpose(left, (2, 0, 1, 3, 4)).reshape(-1, 2 * k)
    right = subtree.reshape(-1, subtree.shape[-1])
    out = jnp.dot(left, right, preferred_element_type=jnp.float32)
    q = lax.reduce_precision(out, exponent_bits=8, mantissa_bits=7)
    q = q.reshape(n_sl, 2, blocks, RB // n_sl, out.shape[-1])
    return lax.all_to_all(q, "sl", 0, 0, tiled=True).sum(axis=0)


def local(stem_cache, subtree_cache, final_gates, group_rows):
    stem = stem_cache[0]
    subtree = subtree_cache[0]
    rows = stem.shape[1]
    half = rows // 2
    n_sa, n_sb, n_sl = lax.axis_size("sa"), lax.axis_size("sb"), lax.axis_size("sl")
    flip = n_sa // 2
    straight = [(i, i ^ flip) for i in range(n_sa)]
    diagonal = [(a * n_sb + b, (a ^ flip) * n_sb + (b ^ 1)) for a in range(n_sa) for b in range(n_sb)]
    cut = rows - rows // 4
    lower = lax.ppermute(stem[:, :half], "sa", straight)
    middle = lax.ppermute(stem[:, half:cut], ("sa", "sb"), diagonal)
    last_src, _, _ = lax.optimization_barrier((stem[:, cut:], lower, middle))
    last = lax.ppermute(last_src, ("sa", "sb"), diagonal)
    first = jnp.concatenate([lower, middle], axis=1)
    q_first = pair_sums(stacked_dot(first, subtree), n_sl)
    q_last = pair_major_sums(last, subtree, n_sl)
    q = jnp.concatenate([q_first, q_last], axis=1)
    wanted = jnp.take(q, group_rows, axis=1)
    chosen = lax.all_to_all(wanted, ("sa", "sb"), 1, 1, tiled=True).sum(axis=1)
    gates = final_gates.astype(jnp.float32)
    out_real, out_imag = complex_dot(chosen[0], chosen[1], gates, precision=lax.Precision.HIGHEST)
    return jnp.concatenate([out_real, out_imag], axis=1)


def solution(mesh):
    return jax.shard_map(
        local,
        mesh=mesh,
        in_specs=(
            P(ALL, None, None, None),
            P(ALL, None, None, None),
            P(),
            P(),
        ),
        out_specs=P(ALL, None),
        check_vma=False,
    )
```

```python
import jax
import jax.numpy as jnp
from jax import lax
from jax.sharding import PartitionSpec as P

RB = 16
ALL = ("sa", "sb", "sl")


def complex_dot(left_real, left_imag, right, precision=None):
    dot = lambda a, b: jnp.dot(a, b, preferred_element_type=jnp.float32, precision=precision)
    real = dot(left_real, right[0]) - dot(left_imag, right[1])
    imag = dot(left_real, right[1]) + dot(left_imag, right[0])
    return (real, imag)


def stacked_dot(stem, subtree):
    rows = stem.shape[1]
    left = jnp.concatenate(
        [jnp.concatenate([stem[0], -stem[1]], axis=1), jnp.concatenate([stem[1], stem[0]], axis=1)], axis=0
    )
    right = subtree.reshape(-1, subtree.shape[-1])
    out = jnp.dot(left, right, preferred_element_type=jnp.float32)
    return out.reshape(2, rows, out.shape[-1])


def pair_sums(partial_s, n_sl):
    blocks = partial_s.shape[1] // RB
    q = lax.reduce_precision(partial_s, exponent_bits=8, mantissa_bits=7)
    q = q.reshape(2, blocks, n_sl, RB // n_sl, partial_s.shape[2])
    return lax.all_to_all(q, "sl", 2, 2, tiled=True).sum(axis=2)


def local(stem_cache, subtree_cache, final_gates, group_rows):
    stem = stem_cache[0]
    subtree = subtree_cache[0]
    rows = stem.shape[1]
    half = rows // 2
    n_sa, n_sb, n_sl = lax.axis_size("sa"), lax.axis_size("sb"), lax.axis_size("sl")
    flip = n_sa // 2
    straight = [(i, i ^ flip) for i in range(n_sa)]
    diagonal = [(a * n_sb + b, (a ^ flip) * n_sb + (b ^ 1)) for a in range(n_sa) for b in range(n_sb)]
    cut = rows - rows // 4
    lower = lax.ppermute(stem[:, :half], "sa", straight)
    middle = lax.ppermute(stem[:, half:cut], ("sa", "sb"), diagonal)
    last_src, _, _ = lax.optimization_barrier((stem[:, cut:], lower, middle))
    last = lax.ppermute(last_src, ("sa", "sb"), diagonal)
    left = jnp.concatenate(
        [
            jnp.concatenate([lower[0], -lower[1]], axis=1),
            jnp.concatenate([middle[0], -middle[1]], axis=1),
            jnp.concatenate([lower[1], lower[0]], axis=1),
            jnp.concatenate([middle[1], middle[0]], axis=1),
        ],
        axis=0,
    )
    first = jnp.dot(left, subtree.reshape(-1, subtree.shape[-1]), preferred_element_type=jnp.float32)
    q_first = pair_sums(first.reshape(2, -1, first.shape[-1]), n_sl)
    q_last = pair_sums(stacked_dot(last, subtree), n_sl)
    q = jnp.concatenate([q_first, q_last], axis=1)
    wanted = jnp.take(q, group_rows, axis=1)
    chosen = lax.all_to_all(wanted, ("sa", "sb"), 1, 1, tiled=True).sum(axis=1)
    gates = final_gates.astype(jnp.float32)
    out_real, out_imag = complex_dot(chosen[0], chosen[1], gates, precision=lax.Precision.HIGHEST)
    return jnp.concatenate([out_real, out_imag], axis=1)


def solution(mesh):
    return jax.shard_map(
        local,
        mesh=mesh,
        in_specs=(
            P(ALL, None, None, None),
            P(ALL, None, None, None),
            P(),
            P(),
        ),
        out_specs=P(ALL, None),
        check_vma=False,
    )
```
